1024 devices in a mesh: expert: 64 (over z, core), dp: 16 (over x, y).
Axes of the slice: x: 4, y: 4, z: 32, core: 2. Of those that a mesh axis runs over, the one named last changes fastest.
Arguments:
- hidden: bfloat16 [16, 64, 64, 8, 768], P('dp', 'expert'), may hold values from -256 to 256, as said below
- expert_ids: int32 [16, 2048, 8], P('dp', 'expert'), may hold values from 0 to 63, all different within a row; in each aligned block of 32 rows (0 to 31, 32 to 63, ..., all dimensions but the last counted through in order) at most 8 rows name the same one
- gate_weights: float32 [16, 2048, 8], P('dp', 'expert'), may hold values from 0.02 to 0.3
- direction: bfloat16 [64, 2048, 768], P('expert'), may hold values from -100 to 100
- solution: float32 [64, 2048, 768], P('expert', 'dp'), may hold values from -6 to 6
- residual: float32 [64, 2048, 768], P('expert', 'dp'), may hold values from -100 to 100
Outputs:
- new_solution: float32 [64, 2048, 768], P('expert', 'dp')
- new_residual: float32 [64, 2048, 768], P('expert', 'dp')
The draws below stay inside these ranges and needn't reach their ends.
Inputs may be any that keep to these rules, and one draw needn't show every extreme that they name: `expert_ids`: in each aligned block of 32 tokens (the tokens of one device), no expert is named by more than 8 rows, a bound that some block reaches; the 8 ids of a token differ. `hidden`: slots that no row names hold values that reach no output.
All inputs are finite; a program needn't handle non-finite values.
Results may differ from the reference program's by a relative error of at most 0.0095.
Values may be sent and summed in bfloat16 or wider, within the bound.
No kernel may reach another device: no remote copies, remote signals or barrier semaphores. Data moves between devices by JAX's collectives and lax.ppermute only.
A program may use at most 32 MiB of HBM per device.

```python
import math
import jax
import jax.numpy as jnp
import numpy as np
from jax import lax

D = 2048
FF = 768
TOP = 8
TOK_DEV = 32
EXPERTS = 64
SOURCES = 64
REPLICAS = 16
TOK_REP = 2048
CAP = 8


def draw_hidden(key, part):
    noise_key = jax.random.fold_in(key, 11)
    row_key = jax.random.fold_in(key, 12)
    column_key = jax.random.fold_in(key, 13)
    heavy_key = jax.random.fold_in(key, 15)
    full_shape = (REPLICAS, EXPERTS, SOURCES, CAP, FF)
    row_scale = jnp.power(10.0, jax.random.uniform(row_key, (REPLICAS, EXPERTS, SOURCES, CAP, 1), jnp.float32) - 0.5)
    column_scale = jnp.power(10.0, jax.random.uniform(column_key, (FF,), jnp.float32) - 0.5)
    heavy_pick = jax.random.uniform(heavy_key, (EXPERTS, SOURCES), jnp.float32) < 0.125
    heavy_scale = jnp.where(heavy_pick, 4.0, 1.0)[None, :, :, None, None]
    values = jax.random.truncated_normal(noise_key, -6.0, 6.0, full_shape, jnp.float32)
    return (values * row_scale * column_scale * heavy_scale).astype(jnp.bfloat16)


def spread_field(key, values, expert_gain, reverse):
    column_key = jax.random.fold_in(key, 22)
    unit_key = jax.random.fold_in(key, 23)
    expert_ramp = jnp.arange(EXPERTS, dtype=jnp.float32) / max(EXPERTS - 1, 1)
    if reverse:
        expert_ramp = 1.0 - expert_ramp
    width_ramp = jnp.arange(D, dtype=jnp.float32) / max(D - 1, 1)
    column_part = jax.random.uniform(column_key, (D,), jnp.float32)
    unit_part = jax.random.uniform(unit_key, (FF,), jnp.float32)
    exponent = expert_gain * expert_ramp[:, None, None] + 0.5 * width_ramp[None, :, None]
    exponent = exponent + 0.5 * (column_part - 0.5)[None, :, None] + (unit_part - 0.5)[None, None, :]
    return 0.3 * values * jnp.power(10.0, exponent)


def field_values(key):
    noise_key = jax.random.fold_in(key, 21)
    full_shape = (EXPERTS, D, FF)
    values = jax.random.truncated_normal(noise_key, -5.0, 5.0, full_shape, jnp.float32)
    return values


def draw_direction(key, part):
    own_key = jax.random.fold_in(key, 31)
    expert_gain = 0.5
    return spread_field(own_key, field_values(own_key), expert_gain, False).astype(jnp.bfloat16)


def draw_residual(key, part):
    own_key = jax.random.fold_in(key, 41)
    expert_gain = 0.5
    return spread_field(own_key, field_values(own_key), expert_gain, True).astype(jnp.float32)


def steps_of(key, shape, split, smallest, largest):
    gain = 1.0
    for position, parts in split:
        draws = jax.random.uniform(jax.random.fold_in(jax.random.fold_in(key, 6), position), (parts,), jnp.float32, smallest / len(split), largest / len(split))
        gain = gain * jnp.repeat(jnp.exp(draws), shape[position] // parts).reshape((-1,) + (1,) * (len(shape) - 1 - position))
    return gain


def shared_out(rng, own, number, rows, number_of, top, most, lean):
    ranking = jax.random.permutation(rng, number_of)
    crowded, usual = load_shares(number_of, rows * top, most, lean, True), load_shares(number_of, rows * top, most, lean, False)
    places = jnp.arange(number_of)

    def named(lengths, turn):
        used = int((lengths > 0).sum())
        fixed = max(1, used // 4)
        moved = fixed + (places - fixed + turn * (used - fixed)) % max(1, number_of - fixed)
        return jnp.zeros((number_of,), jnp.int32).at[ranking[jnp.where(places < fixed, places, moved)]].set(jnp.asarray(lengths, jnp.int32))

    lengths = jnp.where(number % 4 == 0, named(crowded, number // 4), named(usual, number - number // 4 - 1))
    mixed = jax.random.permutation(jax.random.fold_in(own, 3), number_of)
    giver, sink = mixed[0:number_of // 2 * 2:2], mixed[1:number_of // 2 * 2:2]
    slack = jnp.minimum(lengths[giver] - 1, most - lengths[sink]) // 2
    slack = jnp.where((giver == ranking[0]) | (sink == ranking[0]) | (lengths[sink] == 0), 0, jnp.maximum(slack, 0))
    moved = jax.random.randint(jax.random.fold_in(own, 4), (number_of // 2,), 0, 1 << 20) % (slack + 1)
    lengths = lengths.at[giver].add(-moved).at[sink].add(moved)
    members = jnp.searchsorted(jnp.cumsum(lengths), jnp.arange(rows * top), side="right").astype(jnp.int32)
    table = members.reshape(top, rows).T
    table = table[jax.random.permutation(jax.random.fold_in(own, 1), rows)]
    turn = jax.random.randint(jax.random.fold_in(own, 2), (rows, 1), 0, top)
    return jnp.take_along_axis(table, (jnp.arange(top)[None, :] + turn) % top, axis=1)


def load_shares(count, total, reach, skew, full):
    loads = [(1 << 20) // math.isqrt(grade ** skew) + 1 for grade in range(1, count + 1)]
    largest = reach if full else min(reach, max(-(-total // count), total * loads[0] // sum(loads)))
    least = 1 if total - largest >= count - 1 else 0
    given, surplus = [largest] + [least] * (count - 1), total - largest - least * (count - 1)
    while surplus > 0:
        movable = [i for i in range(1, count) if given[i] < largest] or [i for i in range(1, count) if given[i] < reach]
        pool, remaining = sum([loads[i] for i in movable]), surplus
        for i in movable:
            more = min(reach - given[i], max(1, remaining * loads[i] // pool), surplus)
            given[i] = given[i] + more
            surplus = surplus - more
    return np.array(given)


def normal_values(key, dims, spread, bound, cuts=(), held_as=jnp.bfloat16):
    drawn = spread * jax.random.normal(key, dims, jnp.float32)
    if cuts:
        drawn = drawn * steps_of(key, dims, cuts, -0.22, 0.18)
    return jnp.clip(drawn, -bound, bound).astype(held_as)


def setup_inputs(seed: int = 0) -> dict:
    streams_of = jax.random.split(jax.random.key(seed), 7)
    hidden = draw_hidden(jax.random.fold_in(streams_of[6], 71), 0)
    expert_ids_keys = jax.random.split(jax.random.fold_in(streams_of[1], 1), REPLICAS * TOK_REP // TOK_DEV)
    expert_ids_turns = jax.random.permutation(jax.random.fold_in(streams_of[1], 3), REPLICAS * TOK_REP // TOK_DEV)
    expert_ids = jax.vmap(lambda own, number: shared_out(jax.random.fold_in(streams_of[1], 2), own, number, TOK_DEV, EXPERTS, TOP, CAP, 2))(expert_ids_keys, expert_ids_turns).reshape((REPLICAS, TOK_REP, TOP))
    gate_weights = jnp.clip(0.02 + 0.28 * jax.random.uniform(streams_of[2], (REPLICAS, TOK_REP, TOP), jnp.float32) ** steps_of(streams_of[2], (REPLICAS, TOK_REP, TOP), ((0, 16), (1, 64)), -0.2, 0.2), 0.02, 0.3)
    direction = draw_direction(jax.random.fold_in(streams_of[6], 71), 0)
    solution = normal_values(streams_of[4], (EXPERTS, D, FF), 1.0, 6.0, ((0, 64), (1, 16)), jnp.float32)
    residual = draw_residual(jax.random.fold_in(streams_of[6], 71), 0)
    return dict(hidden=hidden, expert_ids=expert_ids, gate_weights=gate_weights, direction=direction, solution=solution, residual=residual)


def slot_numbers(ids_block):
    experts_row = jnp.arange(EXPERTS, dtype=jnp.int32)
    onehot = (ids_block[:, :, None] == experts_row[None, None, :]).astype(jnp.int32)
    earlier = jnp.cumsum(onehot, axis=1) - onehot
    return jnp.sum(earlier * onehot, axis=2).astype(jnp.int32)


def replica_term(hidden_rep, ids_rep, gates_rep, vector):
    ids_block = ids_rep.reshape(SOURCES, TOK_DEV * TOP).astype(jnp.int32)
    slot_index = slot_numbers(ids_block)
    source = jnp.broadcast_to(jnp.arange(SOURCES, dtype=jnp.int32)[:, None], ids_block.shape)
    cached = hidden_rep.astype(jnp.float32)
    row_images = jnp.einsum("escf,edf->escd", cached, vector).astype(jnp.bfloat16)
    row_images = lax.optimization_barrier(row_images)
    picked = row_images[ids_block, source, slot_index].astype(jnp.float32)
    picked = picked.reshape(SOURCES, TOK_DEV, TOP, D)
    gate_rows = gates_rep.reshape(SOURCES, TOK_DEV, TOP)
    tangent = jnp.sum(gate_rows[..., None] * picked, axis=2)
    weighted = (gate_rows[..., None] * tangent[:, :, None, :]).astype(jnp.bfloat16)
    weighted = weighted.reshape(SOURCES, TOK_DEV * TOP, D)
    buffer = jnp.zeros((EXPERTS, SOURCES, CAP, D), jnp.bfloat16)
    buffer = buffer.at[ids_block, source, slot_index].set(weighted)
    buffer = lax.optimization_barrier(buffer)
    partial_value = jnp.einsum("escd,escf->edf", buffer.astype(jnp.float32), cached).astype(jnp.bfloat16)
    partial_value = lax.optimization_barrier(partial_value)
    return partial_value.astype(jnp.float32)


def reference(hidden, expert_ids, gate_weights, direction, solution, residual):
    vector = direction.astype(jnp.float32)

    def accumulate(running, inputs):
        hidden_rep, ids_rep, gates_rep = inputs
        return running + replica_term(hidden_rep, ids_rep, gates_rep, vector), None

    initial = jnp.zeros((EXPERTS, D, FF), jnp.float32)
    running, unused = lax.scan(accumulate, initial, (hidden, expert_ids, gate_weights))
    norm_scale = 1.0 / (REPLICAS * TOK_DEV)
    product = running * norm_scale + vector
    curvature = jnp.sum(vector * product)
    step_size = jnp.sum(residual * residual) / curvature
    return solution + step_size * vector, residual - step_size * product
```

```python
import functools

import jax
import jax.numpy as jnp
from jax import lax
from jax.sharding import Mesh
from jax.sharding import PartitionSpec as P

EXPERT = ("expert_0", "expert_1")
DP = ("dp_0", "dp_1")
EXPERT_DP = ("expert_0", "expert_1", "dp_0", "dp_1")


def over_axes(value, axes):
    return functools.reduce(lax.psum, axes, value)


def split_up(value, dim, count):
    before, after = (value.shape[:dim], value.shape[dim + 1 :])
    return jnp.moveaxis(value.reshape(*before, count, -1, *after), dim, 0)


def sent_and_summed(value, axis, dim):
    count = lax.axis_size(axis)
    blocks = lax.all_to_all(split_up(value, dim, count), axis, 0, 0, tiled=True)
    return jnp.sum(blocks.astype(jnp.float32), axis=0)


def slot_numbers(flat_ids, experts):
    onehot = (flat_ids[:, None] == jnp.arange(experts, dtype=jnp.int32)[None, :]).astype(jnp.int32)
    earlier = jnp.cumsum(onehot, axis=0) - onehot
    return jnp.sum(earlier * onehot, axis=1)


def local(hidden, expert_ids, gate_weights, direction, solution, residual):
    sources = hidden.shape[2]
    capacity = hidden.shape[3]
    hidden_units = hidden.shape[4]
    model_width = direction.shape[1]
    tok_rows = expert_ids.shape[1]
    top_count = expert_ids.shape[2]
    experts = lax.axis_size(EXPERT)
    replicas = lax.axis_size(DP)
    shard_rows = model_width // replicas
    norm_scale = 1.0 / (replicas * tok_rows)
    flat_ids = expert_ids.reshape(tok_rows * top_count)
    position = flat_ids * capacity + slot_numbers(flat_ids, experts)
    cached = hidden.reshape(sources * capacity, hidden_units)
    vector = direction.reshape(model_width, hidden_units)
    offset = lax.axis_index(DP) * shard_rows
    own_rows = lax.dynamic_slice_in_dim(vector, offset, shard_rows, 0).astype(jnp.float32)
    residual_rows = residual.reshape(shard_rows, hidden_units)
    images = lax.dot_general(
        cached, vector, (((1,), (1,)), ((), ())), preferred_element_type=jnp.float32
    )
    images = images.astype(jnp.bfloat16).reshape(sources, capacity, model_width)
    returned = lax.all_to_all(images, EXPERT, split_axis=0, concat_axis=0, tiled=True)
    row_images = returned.reshape(experts * capacity, model_width)[position]
    gate_rows = gate_weights.reshape(tok_rows, top_count)
    tangent = jnp.sum(
        gate_rows[:, :, None] * row_images.reshape(tok_rows, top_count, model_width), axis=1
    )
    weighted = (gate_rows[:, :, None] * tangent[:, None, :]).astype(jnp.bfloat16)
    outgoing = jnp.zeros((experts * capacity, model_width), jnp.bfloat16)
    outgoing = outgoing.at[position].set(weighted.reshape(tok_rows * top_count, model_width))
    local_curvature = norm_scale * jnp.sum(tangent * tangent) + jnp.sum(own_rows * own_rows)
    early_sums = lax.psum(
        jnp.stack([local_curvature, jnp.sum(residual_rows * residual_rows)]), EXPERT_DP
    )
    arrived = lax.all_to_all(
        outgoing.reshape(experts, capacity, model_width),
        EXPERT,
        split_axis=0,
        concat_axis=0,
        tiled=True,
    )
    arrived = arrived.reshape(sources * capacity, model_width)
    summed = sent_and_summed(
        lax.dot_general(
            arrived, cached, (((0,), (0,)), ((), ())), preferred_element_type=jnp.float32
        ).astype(jnp.bfloat16),
        DP,
        0,
    )
    product = summed * norm_scale + own_rows
    step_size = early_sums[1] / early_sums[0]
    new_solution = solution + step_size * own_rows[None]
    new_residual = residual - step_size * product[None]
    return (new_solution, new_residual)


def solution(mesh):
    torus = Mesh(mesh.devices.reshape(32, 2, 4, 4), ("expert_0", "expert_1", "dp_0", "dp_1"))
    return jax.shard_map(
        local,
        mesh=torus,
        in_specs=(
            P(DP, EXPERT, None, None, None),
            P(DP, EXPERT, None),
            P(DP, EXPERT, None),
            P(EXPERT, None, None),
            P(EXPERT, DP, None),
            P(EXPERT, DP, None),
        ),
        out_specs=(P(EXPERT, DP, None), P(EXPERT, DP, None)),
        check_vma=False,
    )
```

```python
import functools

import jax
import jax.numpy as jnp
from jax import lax
from jax.sharding import Mesh
from jax.sharding import PartitionSpec as P

EXPERT = ("expert_0", "expert_1")
DP = ("dp_0", "dp_1")
EXPERT_DP = ("expert_0", "expert_1", "dp_0", "dp_1")


def over_axes(value, axes):
    return functools.reduce(lax.psum, axes, value)


def split_up(value, dim, count):
    before, after = (value.shape[:dim], value.shape[dim + 1 :])
    return jnp.moveaxis(value.reshape(*before, count, -1, *after), dim, 0)


def sent_and_summed(value, axis, dim):
    count = lax.axis_size(axis)
    blocks = lax.all_to_all(split_up(value, dim, count), axis, 0, 0, tiled=True)
    return jnp.sum(blocks.astype(jnp.float32), axis=0)


def slot_numbers(flat_ids, experts):
    onehot = (flat_ids[:, None] == jnp.arange(experts, dtype=jnp.int32)[None, :]).astype(jnp.int32)
    earlier = jnp.cumsum(onehot, axis=0) - onehot
    return jnp.sum(earlier * onehot, axis=1)


def local(hidden, expert_ids, gate_weights, direction, solution, residual):
    sources = hidden.shape[2]
    capacity = hidden.shape[3]
    hidden_units = hidden.shape[4]
    model_width = direction.shape[1]
    tok_rows = expert_ids.shape[1]
    top_count = expert_ids.shape[2]
    experts = lax.axis_size(EXPERT)
    replicas = lax.axis_size(DP)
    shard_rows = model_width // replicas
    norm_scale = 1.0 / (replicas * tok_rows)
    flat_ids = expert_ids.reshape(tok_rows * top_count)
    position = flat_ids * capacity + slot_numbers(flat_ids, experts)
    cached = hidden.reshape(sources * capacity, hidden_units)
    vector = direction.reshape(model_width, hidden_units)
    offset = lax.axis_index(DP) * shard_rows
    own_rows = lax.dynamic_slice_in_dim(vector, offset, shard_rows, 0).astype(jnp.float32)
    residual_rows = residual.reshape(shard_rows, hidden_units)
    images = lax.dot_general(
        cached, vector, (((1,), (1,)), ((), ())), preferred_element_type=jnp.float32
    )
    images = images.astype(jnp.bfloat16).reshape(sources, capacity, model_width)
    returned = lax.all_to_all(images, EXPERT, split_axis=0, concat_axis=0, tiled=True)
    row_images = returned.reshape(experts * capacity, model_width)[position]
    gate_rows = gate_weights.reshape(tok_rows, top_count)
    tangent = jnp.sum(
        gate_rows[:, :, None] * row_images.reshape(tok_rows, top_count, model_width), axis=1
    )
    weighted = (gate_rows[:, :, None] * tangent[:, None, :]).astype(jnp.bfloat16)
    outgoing = jnp.zeros((experts * capacity, model_width), jnp.bfloat16)
    outgoing = outgoing.at[position].set(weighted.reshape(tok_rows * top_count, model_width))
    local_curvature = norm_scale * jnp.sum(tangent * tangent) + jnp.sum(own_rows * own_rows)
    local_sums = jnp.stack([local_curvature, jnp.sum(residual_rows * residual_rows)])
    sums_high = local_sums.astype(jnp.bfloat16)
    sums_low = (local_sums - sums_high.astype(jnp.float32)).astype(jnp.bfloat16)
    lanes = 128
    carried = jnp.zeros((experts, capacity, lanes), jnp.bfloat16)
    carried = carried.at[:, 0, 0:2].set(sums_high).at[:, 0, 2:4].set(sums_low)
    payload = jnp.concatenate(
        [outgoing.reshape(experts, capacity, model_width), carried], axis=2
    )
    arrived_full = lax.all_to_all(payload, EXPERT, split_axis=0, concat_axis=0, tiled=True)
    pieces = arrived_full[:, 0, model_width : model_width + 4].astype(jnp.float32)
    expert_sums = jnp.sum(pieces[:, 0:2] + pieces[:, 2:4], axis=0)
    arrived = arrived_full[:, :, :model_width].reshape(sources * capacity, model_width)
    summed = sent_and_summed(
        lax.dot_general(
            arrived, cached, (((0,), (0,)), ((), ())), preferred_element_type=jnp.float32
        ).astype(jnp.bfloat16),
        DP,
        0,
    )
    early_sums = lax.psum(expert_sums, DP)
    product = summed * norm_scale + own_rows
    step_size = early_sums[1] / early_sums[0]
    new_solution = solution + step_size * own_rows[None]
    new_residual = residual - step_size * product[None]
    return (new_solution, new_residual)


def solution(mesh):
    torus = Mesh(mesh.devices.reshape(32, 2, 4, 4), ("expert_0", "expert_1", "dp_0", "dp_1"))
    return jax.shard_map(
        local,
        mesh=torus,
        in_specs=(
            P(DP, EXPERT, None, None, None),
            P(DP, EXPERT, None),
            P(DP, EXPERT, None),
            P(EXPERT, None, None),
            P(EXPERT, DP, None),
            P(EXPERT, DP, None),
        ),
        out_specs=(P(EXPERT, DP, None), P(EXPERT, DP, None)),
        check_vma=False,
    )
```

```python
import functools

import jax
import jax.numpy as jnp
from jax import lax
from jax.sharding import Mesh
from jax.sharding import PartitionSpec as P

EXPERT = ("expert_0", "expert_1")
DP = ("dp_0", "dp_1")
EXPERT_DP = ("expert_0", "expert_1", "dp_0", "dp_1")


def over_axes(value, axes):
    return functools.reduce(lax.psum, axes, value)


def split_up(value, dim, count):
    before, after = (value.shape[:dim], value.shape[dim + 1 :])
    return jnp.moveaxis(value.reshape(*before, count, -1, *after), dim, 0)


def sent_and_summed(value, axis, dim):
    count = lax.axis_size(axis)
    blocks = lax.all_to_all(split_up(value, dim, count), axis, 0, 0, tiled=True)
    return jnp.sum(blocks.astype(jnp.float32), axis=0)


def slot_numbers(flat_ids, experts):
    onehot = (flat_ids[:, None] == jnp.arange(experts, dtype=jnp.int32)[None, :]).astype(jnp.int32)
    earlier = jnp.cumsum(onehot, axis=0) - onehot
    return jnp.sum(earlier * onehot, axis=1)


def local(hidden, expert_ids, gate_weights, direction, solution, residual):
    sources = hidden.shape[2]
    capacity = hidden.shape[3]
    hidden_units = hidden.shape[4]
    model_width = direction.shape[1]
    tok_rows = expert_ids.shape[1]
    top_count = expert_ids.shape[2]
    experts = lax.axis_size(EXPERT)
    replicas = lax.axis_size(DP)
    shard_rows = model_width // replicas
    norm_scale = 1.0 / (replicas * tok_rows)
    flat_ids = expert_ids.reshape(tok_rows * top_count)
    position = flat_ids * capacity + slot_numbers(flat_ids, experts)
    cached = hidden.reshape(sources * capacity, hidden_units)
    vector = direction.reshape(model_width, hidden_units)
    offset = lax.axis_index(DP) * shard_rows
    own_rows = lax.dynamic_slice_in_dim(vector, offset, shard_rows, 0).astype(jnp.float32)
    residual_rows = residual.reshape(shard_rows, hidden_units)
    images = lax.dot_general(
        cached, vector, (((1,), (1,)), ((), ())), preferred_element_type=jnp.float32
    )
    images = images.astype(jnp.bfloat16).reshape(sources, capacity, model_width)
    returned = lax.all_to_all(images, EXPERT, split_axis=0, concat_axis=0, tiled=True)
    row_images = returned.reshape(experts * capacity, model_width)[position]
    gate_rows = gate_weights.reshape(tok_rows, top_count)
    tangent = jnp.sum(
        gate_rows[:, :, None] * row_images.reshape(tok_rows, top_count, model_width), axis=1
    )
    weighted = (gate_rows[:, :, None] * tangent[:, None, :]).astype(jnp.bfloat16)
    outgoing = jnp.zeros((experts * capacity, model_width), jnp.bfloat16)
    outgoing = outgoing.at[position].set(weighted.reshape(tok_rows * top_count, model_width))
    local_curvature = norm_scale * jnp.sum(tangent * tangent) + jnp.sum(own_rows * own_rows)
    local_sums = jnp.stack([local_curvature, jnp.sum(residual_rows * residual_rows)])
    gathered = lax.all_gather(local_sums, EXPERT, axis=0, tiled=True)
    expert_sums = jnp.sum(gathered.reshape(experts, 2), axis=0)
    arrived = lax.all_to_all(
        outgoing.reshape(experts, capacity, model_width),
        EXPERT,
        split_axis=0,
        concat_axis=0,
        tiled=True,
    )
    arrived = arrived.reshape(sources * capacity, model_width)
    partial_value = lax.dot_general(
        arrived, cached, (((0,), (0,)), ((), ())), preferred_element_type=jnp.float32
    ).astype(jnp.bfloat16)
    totals = lax.psum_scatter(
        jnp.broadcast_to(
            jnp.pad(expert_sums.reshape(1, 1, 2), ((0, 0), (0, 7), (0, 126))), (replicas, 8, 128)
        ).reshape(replicas * 8, 128),
        DP,
        scatter_dimension=0,
        tiled=True,
    )[0, 0:2]
    summed = lax.psum_scatter(
        partial_value.astype(jnp.float32), DP, scatter_dimension=0, tiled=True
    )
    product = summed * norm_scale + own_rows
    step_size = totals[1] / totals[0]
    new_solution = solution + step_size * own_rows[None]
    new_residual = residual - step_size * product[None]
    return (new_solution, new_residual)


def solution(mesh):
    torus = Mesh(mesh.devices.reshape(32, 2, 4, 4), ("expert_0", "expert_1", "dp_0", "dp_1"))
    return jax.shard_map(
        local,
        mesh=torus,
        in_specs=(
            P(DP, EXPERT, None, None, None),
            P(DP, EXPERT, None),
            P(DP, EXPERT, None),
            P(EXPERT, None, None),
            P(EXPERT, DP, None),
            P(EXPERT, DP, None),
        ),
        out_specs=(P(EXPERT, DP, None), P(EXPERT, DP, None)),
        check_vma=False,
    )
```

```python
import functools

import jax
import jax.numpy as jnp
from jax import lax
from jax.sharding import Mesh
from jax.sharding import PartitionSpec as P

EXPERT = ("expert_0", "expert_1")
DP = ("dp_0", "dp_1")
EXPERT_DP = ("expert_0", "expert_1", "dp_0", "dp_1")


def over_axes(value, axes):
    return functools.reduce(lax.psum, axes, value)


def split_up(value, dim, count):
    before, after = (value.shape[:dim], value.shape[dim + 1 :])
    return jnp.moveaxis(value.reshape(*before, count, -1, *after), dim, 0)


def sent_and_summed(value, axis, dim):
    count = lax.axis_size(axis)
    blocks = lax.all_to_all(split_up(value, dim, count), axis, 0, 0, tiled=True)
    return jnp.sum(blocks.astype(jnp.float32), axis=0)


def as_pieces(values):
    high = lax.reduce_precision(values, exponent_bits=8, mantissa_bits=7)
    low = (values - high).astype(jnp.bfloat16)
    return jnp.concatenate([high.astype(jnp.bfloat16), low]).reshape(1, 1, 4)


def from_pieces(received):
    pieces = received.astype(jnp.float32)
    return jnp.sum(pieces[:, 0:2] + pieces[:, 2:4], axis=0)


def slot_numbers(flat_ids, experts):
    onehot = (flat_ids[:, None] == jnp.arange(experts, dtype=jnp.int32)[None, :]).astype(jnp.int32)
    earlier = jnp.cumsum(onehot, axis=0) - onehot
    return jnp.sum(earlier * onehot, axis=1)


def local(hidden, expert_ids, gate_weights, direction, solution, residual):
    sources = hidden.shape[2]
    capacity = hidden.shape[3]
    hidden_units = hidden.shape[4]
    model_width = direction.shape[1]
    tok_rows = expert_ids.shape[1]
    top_count = expert_ids.shape[2]
    experts = lax.axis_size(EXPERT)
    replicas = lax.axis_size(DP)
    shard_rows = model_width // replicas
    norm_scale = 1.0 / (replicas * tok_rows)
    flat_ids = expert_ids.reshape(tok_rows * top_count)
    position = flat_ids * capacity + slot_numbers(flat_ids, experts)
    cached = hidden.reshape(sources * capacity, hidden_units)
    vector = direction.reshape(model_width, hidden_units)
    offset = lax.axis_index(DP) * shard_rows
    own_rows = lax.dynamic_slice_in_dim(vector, offset, shard_rows, 0).astype(jnp.float32)
    residual_rows = residual.reshape(shard_rows, hidden_units)
    images = lax.dot_general(
        cached, vector, (((1,), (1,)), ((), ())), preferred_element_type=jnp.float32
    )
    images = images.astype(jnp.bfloat16).reshape(sources, capacity, model_width)
    returned = lax.all_to_all(images, EXPERT, split_axis=0, concat_axis=0, tiled=True)
    row_images = returned.reshape(experts * capacity, model_width)[position]
    gate_rows = gate_weights.reshape(tok_rows, top_count)
    tangent = jnp.sum(
        gate_rows[:, :, None] * row_images.reshape(tok_rows, top_count, model_width), axis=1
    )
    weighted = (gate_rows[:, :, None] * tangent[:, None, :]).astype(jnp.bfloat16)
    outgoing = jnp.zeros((experts * capacity, model_width), jnp.bfloat16)
    outgoing = outgoing.at[position].set(weighted.reshape(tok_rows * top_count, model_width))
    local_curvature = norm_scale * jnp.sum(tangent * tangent) + jnp.sum(own_rows * own_rows)
    local_sums = jnp.stack([local_curvature, jnp.sum(residual_rows * residual_rows)])
    lanes = 128
    carried = jnp.broadcast_to(
        jnp.pad(as_pieces(local_sums), ((0, 0), (0, capacity - 1), (0, lanes - 4))),
        (experts, capacity, lanes),
    )
    payload = jnp.concatenate([outgoing.reshape(experts, capacity, model_width), carried], axis=2)
    arrived_full = lax.all_to_all(payload, EXPERT, split_axis=0, concat_axis=0, tiled=True)
    expert_sums = from_pieces(arrived_full[:, 0, model_width : model_width + 4])
    arrived = arrived_full[:, :, :model_width].reshape(sources * capacity, model_width)
    partial_value = lax.dot_general(
        arrived, cached, (((0,), (0,)), ((), ())), preferred_element_type=jnp.float32
    ).astype(jnp.bfloat16)
    extra_rows = 16
    extra = jnp.broadcast_to(
        jnp.pad(as_pieces(expert_sums), ((0, 0), (0, extra_rows - 1), (0, hidden_units - 4))),
        (replicas, extra_rows, hidden_units),
    )
    blocks = jnp.concatenate([split_up(partial_value, 0, replicas), extra], axis=1)
    exchanged = lax.all_to_all(blocks, DP, 0, 0, tiled=True)
    summed = jnp.sum(exchanged[:, :shard_rows].astype(jnp.float32), axis=0)
    totals = from_pieces(exchanged[:, shard_rows, 0:4])
    product = summed * norm_scale + own_rows
    step_size = totals[1] / totals[0]
    new_solution = solution + step_size * own_rows[None]
    new_residual = residual - step_size * product[None]
    return (new_solution, new_residual)


def solution(mesh):
    torus = Mesh(mesh.devices.reshape(32, 2, 4, 4), ("expert_0", "expert_1", "dp_0", "dp_1"))
    return jax.shard_map(
        local,
        mesh=torus,
        in_specs=(
            P(DP, EXPERT, None, None, None),
            P(DP, EXPERT, None),
            P(DP, EXPERT, None),
            P(EXPERT, None, None),
            P(EXPERT, DP, None),
            P(EXPERT, DP, None),
        ),
        out_specs=(P(EXPERT, DP, None), P(EXPERT, DP, None)),
        check_vma=False,
    )
```

```python
import functools

import jax
import jax.numpy as jnp
from jax import lax
from jax.sharding import Mesh
from jax.sharding import PartitionSpec as P

EXPERT = ("expert_0", "expert_1")
DP = ("dp_0", "dp_1")
EXPERT_DP = ("expert_0", "expert_1", "dp_0", "dp_1")


def over_axes(value, axes):
    return functools.reduce(lax.psum, axes, value)


def split_up(value, dim, count):
    before, after = (value.shape[:dim], value.shape[dim + 1 :])
    return jnp.moveaxis(value.reshape(*before, count, -1, *after), dim, 0)


def sent_and_summed(value, axis, dim):
    count = lax.axis_size(axis)
    blocks = lax.all_to_all(split_up(value, dim, count), axis, 0, 0, tiled=True)
    return jnp.sum(blocks.astype(jnp.float32), axis=0)


def as_pieces(values):
    high = lax.reduce_precision(values, exponent_bits=8, mantissa_bits=7)
    low = (values - high).astype(jnp.bfloat16)
    return jnp.concatenate([high.astype(jnp.bfloat16), low]).reshape(1, 1, 4)


def from_pieces(received):
    pieces = received.astype(jnp.float32)
    return jnp.sum(pieces[:, 0:2] + pieces[:, 2:4], axis=0)


def dp_sum(blocks, sides):
    me = lax.axis_index(DP)
    count = sides[0] * sides[1]
    total = lax.dynamic_index_in_dim(blocks, me, 0, keepdims=False).astype(jnp.float32)
    for step in range(1, count):
        first, second = divmod(step, sides[1])
        pairs = []
        for source in range(count):
            row, col = divmod(source, sides[1])
            target = ((row + first) % sides[0]) * sides[1] + (col + second) % sides[1]
            pairs.append((source, target))
        target_of_me = dict(pairs)
        goes = jnp.asarray([target_of_me[i] for i in range(count)], jnp.int32)[me]
        sent = lax.dynamic_index_in_dim(blocks, goes, 0, keepdims=False)
        total = total + lax.ppermute(sent, DP, pairs).astype(jnp.float32)
    return total


def slot_numbers(flat_ids, experts):
    onehot = (flat_ids[:, None] == jnp.arange(experts, dtype=jnp.int32)[None, :]).astype(jnp.int32)
    earlier = jnp.cumsum(onehot, axis=0) - onehot
    return jnp.sum(earlier * onehot, axis=1)


def local(hidden, expert_ids, gate_weights, direction, solution, residual):
    sources = hidden.shape[2]
    capacity = hidden.shape[3]
    hidden_units = hidden.shape[4]
    model_width = direction.shape[1]
    tok_rows = expert_ids.shape[1]
    top_count = expert_ids.shape[2]
    experts = lax.axis_size(EXPERT)
    replicas = lax.axis_size(DP)
    shard_rows = model_width // replicas
    norm_scale = 1.0 / (replicas * tok_rows)
    flat_ids = expert_ids.reshape(tok_rows * top_count)
    position = flat_ids * capacity + slot_numbers(flat_ids, experts)
    cached = hidden.reshape(sources * capacity, hidden_units)
    vector = direction.reshape(model_width, hidden_units)
    offset = lax.axis_index(DP) * shard_rows
    own_rows = lax.dynamic_slice_in_dim(vector, offset, shard_rows, 0).astype(jnp.float32)
    residual_rows = residual.reshape(shard_rows, hidden_units)
    images = lax.dot_general(
        cached, vector, (((1,), (1,)), ((), ())), preferred_element_type=jnp.float32
    )
    images = images.astype(jnp.bfloat16).reshape(sources, capacity, model_width)
    returned = lax.all_to_all(images, EXPERT, split_axis=0, concat_axis=0, tiled=True)
    row_images = returned.reshape(experts * capacity, model_width)[position]
    gate_rows = gate_weights.reshape(tok_rows, top_count)
    tangent = jnp.sum(
        gate_rows[:, :, None] * row_images.reshape(tok_rows, top_count, model_width), axis=1
    )
    weighted = (gate_rows[:, :, None] * tangent[:, None, :]).astype(jnp.bfloat16)
    outgoing = jnp.zeros((experts * capacity, model_width), jnp.bfloat16)
    outgoing = outgoing.at[position].set(weighted.reshape(tok_rows * top_count, model_width))
    local_curvature = norm_scale * jnp.sum(tangent * tangent) + jnp.sum(own_rows * own_rows)
    local_sums = jnp.stack([local_curvature, jnp.sum(residual_rows * residual_rows)])
    lanes = 128
    carried = jnp.broadcast_to(
        jnp.pad(as_pieces(local_sums), ((0, 0), (0, capacity - 1), (0, lanes - 4))),
        (experts, capacity, lanes),
    )
    payload = jnp.concatenate([outgoing.reshape(experts, capacity, model_width), carried], axis=2)
    arrived_full = lax.all_to_all(payload, EXPERT, split_axis=0, concat_axis=0, tiled=True)
    expert_sums = from_pieces(arrived_full[:, 0, model_width : model_width + 4])
    arrived = arrived_full[:, :, :model_width].reshape(sources * capacity, model_width)
    partial_value = lax.dot_general(
        arrived, cached, (((0,), (0,)), ((), ())), preferred_element_type=jnp.float32
    ).astype(jnp.bfloat16)
    extra_rows = 16
    extra = jnp.broadcast_to(
        jnp.pad(as_pieces(expert_sums), ((0, 0), (0, extra_rows - 1), (0, hidden_units - 4))),
        (replicas, extra_rows, hidden_units),
    )
    split_rows = shard_rows // 2
    grouped = split_up(partial_value, 0, replicas)
    blocks = jnp.concatenate([grouped[:, split_rows:], extra], axis=1)
    exchanged = lax.all_to_all(blocks, DP, 0, 0, tiled=True)
    permuted = dp_sum(grouped[:, :split_rows], (lax.axis_size(DP[0]), lax.axis_size(DP[1])))
    summed = jnp.concatenate(
        [permuted, jnp.sum(exchanged[:, : shard_rows - split_rows].astype(jnp.float32), axis=0)],
        axis=0,
    )
    totals = from_pieces(exchanged[:, shard_rows - split_rows, 0:4])
    product = summed * norm_scale + own_rows
    step_size = totals[1] / totals[0]
    new_solution = solution + step_size * own_rows[None]
    new_residual = residual - step_size * product[None]
    return (new_solution, new_residual)


def solution(mesh):
    torus = Mesh(mesh.devices.reshape(32, 2, 4, 4), ("expert_0", "expert_1", "dp_0", "dp_1"))
    return jax.shard_map(
        local,
        mesh=torus,
        in_specs=(
            P(DP, EXPERT, None, None, None),
            P(DP, EXPERT, None),
            P(DP, EXPERT, None),
            P(EXPERT, None, None),
            P(EXPERT, DP, None),
            P(EXPERT, DP, None),
        ),
        out_specs=(P(EXPERT, DP, None), P(EXPERT, DP, None)),
        check_vma=False,
    )
```

```python
import functools

import jax
import jax.numpy as jnp
from jax import lax
from jax.sharding import Mesh
from jax.sharding import PartitionSpec as P

EXPERT = ("expert_0", "expert_1")
DP = ("dp_0", "dp_1")
EXPERT_DP = ("expert_0", "expert_1", "dp_0", "dp_1")


def over_axes(value, axes):
    return functools.reduce(lax.psum, axes, value)


def split_up(value, dim, count):
    before, after = (value.shape[:dim], value.shape[dim + 1 :])
    return jnp.moveaxis(value.reshape(*before, count, -1, *after), dim, 0)


def sent_and_summed(value, axis, dim):
    count = lax.axis_size(axis)
    blocks = lax.all_to_all(split_up(value, dim, count), axis, 0, 0, tiled=True)
    return jnp.sum(blocks.astype(jnp.float32), axis=0)


def as_pieces(values):
    high = lax.reduce_precision(values, exponent_bits=8, mantissa_bits=7)
    low = (values - high).astype(jnp.bfloat16)
    return jnp.concatenate([high.astype(jnp.bfloat16), low]).reshape(1, 1, 4)


def from_pieces(received):
    pieces = received.astype(jnp.float32)
    return jnp.sum(pieces[:, 0:2] + pieces[:, 2:4], axis=0)


def slot_numbers(flat_ids, experts):
    onehot = (flat_ids[:, None] == jnp.arange(experts, dtype=jnp.int32)[None, :]).astype(jnp.int32)
    earlier = jnp.cumsum(onehot, axis=0) - onehot
    return jnp.sum(earlier * onehot, axis=1)


def local(hidden, expert_ids, gate_weights, direction, solution, residual):
    sources = hidden.shape[2]
    capacity = hidden.shape[3]
    hidden_units = hidden.shape[4]
    model_width = direction.shape[1]
    tok_rows = expert_ids.shape[1]
    top_count = expert_ids.shape[2]
    experts = lax.axis_size(EXPERT)
    replicas = lax.axis_size(DP)
    shard_rows = model_width // replicas
    norm_scale = 1.0 / (replicas * tok_rows)
    flat_ids = expert_ids.reshape(tok_rows * top_count)
    position = flat_ids * capacity + slot_numbers(flat_ids, experts)
    cached = hidden.reshape(sources * capacity, hidden_units)
    vector = direction.reshape(model_width, hidden_units)
    offset = lax.axis_index(DP) * shard_rows
    own_rows = lax.dynamic_slice_in_dim(vector, offset, shard_rows, 0).astype(jnp.float32)
    residual_rows = residual.reshape(shard_rows, hidden_units)
    images = lax.dot_general(
        cached, vector, (((1,), (1,)), ((), ())), preferred_element_type=jnp.float32
    )
    images = images.astype(jnp.bfloat16).reshape(sources, capacity, model_width)
    returned = lax.all_to_all(images, EXPERT, split_axis=0, concat_axis=0, tiled=True)
    row_images = returned.reshape(experts * capacity, model_width)[position]
    gate_rows = gate_weights.reshape(tok_rows, top_count)
    tangent = jnp.sum(
        gate_rows[:, :, None] * row_images.reshape(tok_rows, top_count, model_width), axis=1
    )
    weighted = (gate_rows[:, :, None] * tangent[:, None, :]).astype(jnp.bfloat16)
    outgoing = jnp.zeros((experts * capacity, model_width), jnp.bfloat16)
    outgoing = outgoing.at[position].set(weighted.reshape(tok_rows * top_count, model_width))
    local_curvature = norm_scale * jnp.sum(tangent * tangent) + jnp.sum(own_rows * own_rows)
    local_sums = jnp.stack([local_curvature, jnp.sum(residual_rows * residual_rows)])
    lanes = 128
    carried = jnp.broadcast_to(
        jnp.pad(as_pieces(local_sums), ((0, 0), (0, capacity - 1), (0, lanes - 4))),
        (experts, capacity, lanes),
    )
    payload = jnp.concatenate([outgoing.reshape(experts, capacity, model_width), carried], axis=2)
    arrived_full = lax.all_to_all(payload, EXPERT, split_axis=0, concat_axis=0, tiled=True)
    expert_sums = from_pieces(arrived_full[:, 0, model_width : model_width + 4])
    arrived = arrived_full[:, :, :model_width].reshape(sources * capacity, model_width)
    partial_value = lax.dot_general(
        arrived, cached, (((0,), (0,)), ((), ())), preferred_element_type=jnp.float32
    ).astype(jnp.bfloat16)
    extra_rows = 8
    extra = jnp.broadcast_to(
        jnp.pad(as_pieces(expert_sums), ((0, 0), (0, extra_rows - 1), (0, hidden_units - 4))),
        (replicas, extra_rows, hidden_units),
    )
    blocks = jnp.concatenate([split_up(partial_value, 0, replicas), extra], axis=1)
    exchanged = lax.all_to_all(blocks, DP, 0, 0, tiled=True)
    summed = jnp.sum(exchanged[:, :shard_rows].astype(jnp.float32), axis=0)
    totals = from_pieces(exchanged[:, shard_rows, 0:4])
    product = summed * norm_scale + own_rows
    step_size = totals[1] / totals[0]
    new_solution = solution + step_size * own_rows[None]
    new_residual = residual - step_size * product[None]
    return (new_solution, new_residual)


def solution(mesh):
    torus = Mesh(mesh.devices.reshape(32, 2, 4, 4), ("expert_0", "expert_1", "dp_0", "dp_1"))
    return jax.shard_map(
        local,
        mesh=torus,
        in_specs=(
            P(DP, EXPERT, None, None, None),
            P(DP, EXPERT, None),
            P(DP, EXPERT, None),
            P(EXPERT, None, None),
            P(EXPERT, DP, None),
            P(EXPERT, DP, None),
        ),
        out_specs=(P(EXPERT, DP, None), P(EXPERT, DP, None)),
        check_vma=False,
    )
```

```python
import functools

import jax
import jax.numpy as jnp
from jax import lax
from jax.sharding import Mesh
from jax.sharding import PartitionSpec as P

EXPERT = ("expert_0", "expert_1")
DP = ("dp_0", "dp_1")
EXPERT_DP = ("expert_0", "expert_1", "dp_0", "dp_1")


def over_axes(value, axes):
    return functools.reduce(lax.psum, axes, value)


def split_up(value, dim, count):
    before, after = (value.shape[:dim], value.shape[dim + 1 :])
    return jnp.moveaxis(value.reshape(*before, count, -1, *after), dim, 0)


def sent_and_summed(value, axis, dim):
    count = lax.axis_size(axis)
    blocks = lax.all_to_all(split_up(value, dim, count), axis, 0, 0, tiled=True)
    return jnp.sum(blocks.astype(jnp.float32), axis=0)


def as_pieces(values):
    high = lax.reduce_precision(values, exponent_bits=8, mantissa_bits=7)
    low = (values - high).astype(jnp.bfloat16)
    return jnp.concatenate([high.astype(jnp.bfloat16), low]).reshape(1, 1, 4)


def from_pieces(received):
    pieces = received.astype(jnp.float32)
    return jnp.sum(pieces[:, 0:2] + pieces[:, 2:4], axis=0)


def slot_numbers(flat_ids, experts):
    onehot = (flat_ids[:, None] == jnp.arange(experts, dtype=jnp.int32)[None, :]).astype(jnp.int32)
    earlier = jnp.cumsum(onehot, axis=0) - onehot
    return jnp.sum(earlier * onehot, axis=1)


def local(hidden, expert_ids, gate_weights, direction, solution, residual):
    sources = hidden.shape[2]
    capacity = hidden.shape[3]
    hidden_units = hidden.shape[4]
    model_width = direction.shape[1]
    tok_rows = expert_ids.shape[1]
    top_count = expert_ids.shape[2]
    experts = lax.axis_size(EXPERT)
    replicas = lax.axis_size(DP)
    shard_rows = model_width // replicas
    norm_scale = 1.0 / (replicas * tok_rows)
    flat_ids = expert_ids.reshape(tok_rows * top_count)
    position = flat_ids * capacity + slot_numbers(flat_ids, experts)
    cached = hidden.reshape(sources * capacity, hidden_units)
    vector = direction.reshape(model_width, hidden_units)
    offset = lax.axis_index(DP) * shard_rows
    own_rows = lax.dynamic_slice_in_dim(vector, offset, shard_rows, 0).astype(jnp.float32)
    residual_rows = residual.reshape(shard_rows, hidden_units)
    images = lax.dot_general(
        cached, vector, (((1,), (1,)), ((), ())), preferred_element_type=jnp.float32
    )
    images = images.astype(jnp.bfloat16).reshape(sources, capacity, model_width)
    returned = lax.all_to_all(images, EXPERT, split_axis=0, concat_axis=0, tiled=True)
    row_images = returned.reshape(experts * capacity, model_width)[position]
    gate_rows = gate_weights.reshape(tok_rows, top_count)
    tangent = jnp.sum(
        gate_rows[:, :, None] * row_images.reshape(tok_rows, top_count, model_width), axis=1
    )
    weighted = (gate_rows[:, :, None] * tangent[:, None, :]).astype(jnp.bfloat16)
    outgoing = jnp.zeros((experts * capacity, model_width), jnp.bfloat16)
    outgoing = outgoing.at[position].set(weighted.reshape(tok_rows * top_count, model_width))
    local_curvature = norm_scale * jnp.sum(tangent * tangent) + jnp.sum(own_rows * own_rows)
    local_sums = jnp.stack([local_curvature, jnp.sum(residual_rows * residual_rows)])
    lanes = 128
    carried = jnp.broadcast_to(
        jnp.pad(as_pieces(local_sums), ((0, 0), (0, capacity - 1), (0, lanes - 4))),
        (experts, capacity, lanes),
    )
    halves = 2
    half_rows = shard_rows // halves
    width = replicas * half_rows
    split_out = outgoing.reshape(experts, capacity, replicas, halves, half_rows)
    first = split_out[:, :, :, 0].reshape(experts, capacity, width)
    second = split_out[:, :, :, 1].reshape(experts, capacity, width)
    arrived_first = lax.all_to_all(first, EXPERT, split_axis=0, concat_axis=0, tiled=True)
    partial_first = lax.dot_general(
        arrived_first.reshape(sources * capacity, width),
        cached,
        (((0,), (0,)), ((), ())),
        preferred_element_type=jnp.float32,
    ).astype(jnp.bfloat16)
    summed_first = lax.psum_scatter(
        partial_first.astype(jnp.float32), DP, scatter_dimension=0, tiled=True
    )
    payload = jnp.concatenate([second, carried], axis=2)
    arrived_full = lax.all_to_all(payload, EXPERT, split_axis=0, concat_axis=0, tiled=True)
    expert_sums = from_pieces(arrived_full[:, 0, width : width + 4])
    arrived = arrived_full[:, :, :width].reshape(sources * capacity, width)
    partial_value = lax.dot_general(
        arrived, cached, (((0,), (0,)), ((), ())), preferred_element_type=jnp.float32
    ).astype(jnp.bfloat16)
    extra_rows = 8
    extra = jnp.broadcast_to(
        jnp.pad(as_pieces(expert_sums), ((0, 0), (0, extra_rows - 1), (0, hidden_units - 4))),
        (replicas, extra_rows, hidden_units),
    )
    blocks = jnp.concatenate([split_up(partial_value, 0, replicas), extra], axis=1)
    exchanged = lax.all_to_all(blocks, DP, 0, 0, tiled=True)
    summed_second = jnp.sum(exchanged[:, :half_rows].astype(jnp.float32), axis=0)
    totals = from_pieces(exchanged[:, half_rows, 0:4])
    summed = jnp.stack([summed_first, summed_second], axis=0).reshape(shard_rows, hidden_units)
    product = summed * norm_scale + own_rows
    step_size = totals[1] / totals[0]
    new_solution = solution + step_size * own_rows[None]
    new_residual = residual - step_size * product[None]
    return (new_solution, new_residual)


def solution(mesh):
    torus = Mesh(mesh.devices.reshape(32, 2, 4, 4), ("expert_0", "expert_1", "dp_0", "dp_1"))
    return jax.shard_map(
        local,
        mesh=torus,
        in_specs=(
            P(DP, EXPERT, None, None, None),
            P(DP, EXPERT, None),
            P(DP, EXPERT, None),
            P(EXPERT, None, None),
            P(EXPERT, DP, None),
            P(EXPERT, DP, None),
        ),
        out_specs=(P(EXPERT, DP, None), P(EXPERT, DP, None)),
        check_vma=False,
    )
```

```python
import functools

import jax
import jax.numpy as jnp
from jax import lax
from jax.sharding import Mesh
from jax.sharding import PartitionSpec as P

EXPERT = ("expert_0", "expert_1")
DP = ("dp_0", "dp_1")
EXPERT_DP = ("expert_0", "expert_1", "dp_0", "dp_1")


def over_axes(value, axes):
    return functools.reduce(lax.psum, axes, value)


def split_up(value, dim, count):
    before, after = (value.shape[:dim], value.shape[dim + 1 :])
    return jnp.moveaxis(value.reshape(*before, count, -1, *after), dim, 0)


def sent_and_summed(value, axis, dim):
    count = lax.axis_size(axis)
    blocks = lax.all_to_all(split_up(value, dim, count), axis, 0, 0, tiled=True)
    return jnp.sum(blocks.astype(jnp.float32), axis=0)


def as_pieces(values):
    high = lax.reduce_precision(values, exponent_bits=8, mantissa_bits=7)
    low = (values - high).astype(jnp.bfloat16)
    return jnp.concatenate([high.astype(jnp.bfloat16), low]).reshape(1, 1, 4)


def from_pieces(received):
    pieces = received.astype(jnp.float32)
    return jnp.sum(pieces[:, 0:2] + pieces[:, 2:4], axis=0)


def slot_numbers(flat_ids, experts):
    onehot = (flat_ids[:, None] == jnp.arange(experts, dtype=jnp.int32)[None, :]).astype(jnp.int32)
    earlier = jnp.cumsum(onehot, axis=0) - onehot
    return jnp.sum(earlier * onehot, axis=1)


def local(hidden, expert_ids, gate_weights, direction, solution, residual):
    sources = hidden.shape[2]
    capacity = hidden.shape[3]
    hidden_units = hidden.shape[4]
    model_width = direction.shape[1]
    tok_rows = expert_ids.shape[1]
    top_count = expert_ids.shape[2]
    experts = lax.axis_size(EXPERT)
    replicas = lax.axis_size(DP)
    shard_rows = model_width // replicas
    norm_scale = 1.0 / (replicas * tok_rows)
    flat_ids = expert_ids.reshape(tok_rows * top_count)
    position = flat_ids * capacity + slot_numbers(flat_ids, experts)
    cached = hidden.reshape(sources * capacity, hidden_units)
    vector = direction.reshape(model_width, hidden_units)
    offset = lax.axis_index(DP) * shard_rows
    own_rows = lax.dynamic_slice_in_dim(vector, offset, shard_rows, 0).astype(jnp.float32)
    residual_rows = residual.reshape(shard_rows, hidden_units)
    images = lax.dot_general(
        cached, vector, (((1,), (1,)), ((), ())), preferred_element_type=jnp.float32
    )
    images = images.astype(jnp.bfloat16).reshape(sources, capacity, model_width)
    returned = lax.all_to_all(images, EXPERT, split_axis=0, concat_axis=0, tiled=True)
    selector = (
        position[:, None] == jnp.arange(experts * capacity, dtype=jnp.int32)[None, :]
    ).astype(jnp.bfloat16)
    row_images = lax.dot_general(
        selector,
        returned.reshape(experts * capacity, model_width),
        (((1,), (0,)), ((), ())),
        preferred_element_type=jnp.float32,
    )
    gate_rows = gate_weights.reshape(tok_rows, top_count)
    tangent = jnp.sum(
        gate_rows[:, :, None] * row_images.reshape(tok_rows, top_count, model_width), axis=1
    )
    weighted = (gate_rows[:, :, None] * tangent[:, None, :]).astype(jnp.bfloat16)
    outgoing = lax.dot_general(
        selector,
        weighted.reshape(tok_rows * top_count, model_width),
        (((0,), (0,)), ((), ())),
        preferred_element_type=jnp.float32,
    ).astype(jnp.bfloat16)
    local_curvature = norm_scale * jnp.sum(tangent * tangent) + jnp.sum(own_rows * own_rows)
    local_sums = jnp.stack([local_curvature, jnp.sum(residual_rows * residual_rows)])
    lanes = 128
    carried = jnp.broadcast_to(
        jnp.pad(as_pieces(local_sums), ((0, 0), (0, capacity - 1), (0, lanes - 4))),
        (experts, capacity, lanes),
    )
    payload = jnp.concatenate([outgoing.reshape(experts, capacity, model_width), carried], axis=2)
    arrived_full = lax.all_to_all(payload, EXPERT, split_axis=0, concat_axis=0, tiled=True)
    expert_sums = from_pieces(arrived_full[:, 0, model_width : model_width + 4])
    arrived = arrived_full[:, :, :model_width].reshape(sources * capacity, model_width)
    partial_value = lax.dot_general(
        arrived, cached, (((0,), (0,)), ((), ())), preferred_element_type=jnp.float32
    ).astype(jnp.bfloat16)
    extra_rows = 8
    extra = jnp.broadcast_to(
        jnp.pad(as_pieces(expert_sums), ((0, 0), (0, extra_rows - 1), (0, hidden_units - 4))),
        (replicas, extra_rows, hidden_units),
    )
    blocks = jnp.concatenate([split_up(partial_value, 0, replicas), extra], axis=1)
    exchanged = lax.all_to_all(blocks, DP, 0, 0, tiled=True)
    summed = jnp.sum(exchanged[:, :shard_rows].astype(jnp.float32), axis=0)
    totals = from_pieces(exchanged[:, shard_rows, 0:4])
    product = summed * norm_scale + own_rows
    step_size = totals[1] / totals[0]
    new_solution = solution + step_size * own_rows[None]
    new_residual = residual - step_size * product[None]
    return (new_solution, new_residual)


def solution(mesh):
    torus = Mesh(mesh.devices.reshape(32, 2, 4, 4), ("expert_0", "expert_1", "dp_0", "dp_1"))
    return jax.shard_map(
        local,
        mesh=torus,
        in_specs=(
            P(DP, EXPERT, None, None, None),
            P(DP, EXPERT, None),
            P(DP, EXPERT, None),
            P(EXPERT, None, None),
            P(EXPERT, DP, None),
            P(EXPERT, DP, None),
        ),
        out_specs=(P(EXPERT, DP, None), P(EXPERT, DP, None)),
        check_vma=False,
    )
```

```python
import functools

import jax
import jax.numpy as jnp
from jax import lax
from jax.sharding import Mesh
from jax.sharding import PartitionSpec as P

EXPERT = ("expert_0", "expert_1")
DP = ("dp_0", "dp_1")
EXPERT_DP = ("expert_0", "expert_1", "dp_0", "dp_1")


def over_axes(value, axes):
    return functools.reduce(lax.psum, axes, value)


def split_up(value, dim, count):
    before, after = (value.shape[:dim], value.shape[dim + 1 :])
    return jnp.moveaxis(value.reshape(*before, count, -1, *after), dim, 0)


def sent_and_summed(value, axis, dim):
    count = lax.axis_size(axis)
    blocks = lax.all_to_all(split_up(value, dim, count), axis, 0, 0, tiled=True)
    return jnp.sum(blocks.astype(jnp.float32), axis=0)


def as_pieces(values):
    high = lax.reduce_precision(values, exponent_bits=8, mantissa_bits=7)
    low = (values - high).astype(jnp.bfloat16)
    return jnp.concatenate([high.astype(jnp.bfloat16), low]).reshape(1, 1, 4)


def from_pieces(received):
    pieces = received.astype(jnp.float32)
    return jnp.sum(pieces[:, 0:2] + pieces[:, 2:4], axis=0)


def slot_numbers(flat_ids, experts):
    onehot = (flat_ids[:, None] == jnp.arange(experts, dtype=jnp.int32)[None, :]).astype(jnp.int32)
    earlier = jnp.cumsum(onehot, axis=0) - onehot
    return jnp.sum(earlier * onehot, axis=1)


def local(hidden, expert_ids, gate_weights, direction, solution, residual):
    sources = hidden.shape[2]
    capacity = hidden.shape[3]
    hidden_units = hidden.shape[4]
    model_width = direction.shape[1]
    tok_rows = expert_ids.shape[1]
    top_count = expert_ids.shape[2]
    experts = lax.axis_size(EXPERT)
    replicas = lax.axis_size(DP)
    shard_rows = model_width // replicas
    norm_scale = 1.0 / (replicas * tok_rows)
    flat_ids = expert_ids.reshape(tok_rows * top_count)
    position = flat_ids * capacity + slot_numbers(flat_ids, experts)
    cached = hidden.reshape(sources * capacity, hidden_units)
    vector = direction.reshape(model_width, hidden_units)
    offset = lax.axis_index(DP) * shard_rows
    own_rows = lax.dynamic_slice_in_dim(vector, offset, shard_rows, 0).astype(jnp.float32)
    residual_rows = residual.reshape(shard_rows, hidden_units)
    images = lax.dot_general(
        cached, vector, (((1,), (1,)), ((), ())), preferred_element_type=jnp.float32
    )
    images = images.astype(jnp.bfloat16).reshape(sources, capacity, model_width)
    returned = lax.all_to_all(images, EXPERT, split_axis=0, concat_axis=0, tiled=True)
    selector = (
        position[:, None] == jnp.arange(experts * capacity, dtype=jnp.int32)[None, :]
    ).astype(jnp.bfloat16)
    row_images = lax.dot_general(
        selector,
        returned.reshape(experts * capacity, model_width),
        (((1,), (0,)), ((), ())),
        preferred_element_type=jnp.float32,
    )
    gate_rows = gate_weights.reshape(tok_rows, top_count)
    tangent = jnp.sum(
        gate_rows[:, :, None] * row_images.reshape(tok_rows, top_count, model_width), axis=1
    )
    weighted = (gate_rows[:, :, None] * tangent[:, None, :]).astype(jnp.bfloat16)
    outgoing = lax.dot_general(
        selector,
        weighted.reshape(tok_rows * top_count, model_width),
        (((0,), (0,)), ((), ())),
        preferred_element_type=jnp.float32,
    ).astype(jnp.bfloat16)
    local_curvature = norm_scale * jnp.sum(tangent * tangent) + jnp.sum(own_rows * own_rows)
    local_sums = jnp.stack([local_curvature, jnp.sum(residual_rows * residual_rows)])
    lanes = 128
    carried = jnp.broadcast_to(
        jnp.pad(as_pieces(local_sums), ((0, 0), (0, capacity - 1), (0, lanes - 4))),
        (experts, capacity, lanes),
    )
    payload = jnp.concatenate([outgoing.reshape(experts, capacity, model_width), carried], axis=2)
    arrived_full = lax.all_to_all(payload, EXPERT, split_axis=0, concat_axis=0, tiled=True)
    expert_sums = from_pieces(arrived_full[:, 0, model_width : model_width + 4])
    arrived = arrived_full[:, :, :model_width].reshape(sources * capacity, model_width)
    partial_value = lax.dot_general(
        arrived, cached, (((0,), (0,)), ((), ())), preferred_element_type=jnp.float32
    ).astype(jnp.bfloat16)
    extra_rows = 8
    extra = jnp.broadcast_to(
        jnp.pad(as_pieces(expert_sums), ((0, 0), (0, extra_rows - 1), (0, hidden_units - 4))),
        (replicas, extra_rows, hidden_units),
    )
    blocks = jnp.concatenate([split_up(partial_value, 0, replicas), extra], axis=1)
    exchanged = lax.all_to_all(blocks, DP, 0, 0, tiled=True)
    summed = functools.reduce(
        jnp.add, [exchanged[i, :shard_rows].astype(jnp.float32) for i in range(replicas)]
    )
    totals = from_pieces(exchanged[:, shard_rows, 0:4])
    product = summed * norm_scale + own_rows
    step_size = totals[1] / totals[0]
    new_solution = solution + step_size * own_rows[None]
    new_residual = residual - step_size * product[None]
    return (new_solution, new_residual)


def solution(mesh):
    torus = Mesh(mesh.devices.reshape(32, 2, 4, 4), ("expert_0", "expert_1", "dp_0", "dp_1"))
    return jax.shard_map(
        local,
        mesh=torus,
        in_specs=(
            P(DP, EXPERT, None, None, None),
            P(DP, EXPERT, None),
            P(DP, EXPERT, None),
            P(EXPERT, None, None),
            P(EXPERT, DP, None),
            P(EXPERT, DP, None),
        ),
        out_specs=(P(EXPERT, DP, None), P(EXPERT, DP, None)),
        check_vma=False,
    )
```

```python
import functools

import jax
import jax.numpy as jnp
from jax import lax
from jax.sharding import Mesh
from jax.sharding import PartitionSpec as P

EXPERT = ("expert_0", "expert_1")
DP = ("dp_0", "dp_1")
EXPERT_DP = ("expert_0", "expert_1", "dp_0", "dp_1")


def over_axes(value, axes):
    return functools.reduce(lax.psum, axes, value)


def split_up(value, dim, count):
    before, after = (value.shape[:dim], value.shape[dim + 1 :])
    return jnp.moveaxis(value.reshape(*before, count, -1, *after), dim, 0)


def sent_and_summed(value, axis, dim):
    count = lax.axis_size(axis)
    blocks = lax.all_to_all(split_up(value, dim, count), axis, 0, 0, tiled=True)
    return jnp.sum(blocks.astype(jnp.float32), axis=0)


def as_pieces(values):
    high = lax.reduce_precision(values, exponent_bits=8, mantissa_bits=7)
    low = (values - high).astype(jnp.bfloat16)
    return jnp.concatenate([high.astype(jnp.bfloat16), low]).reshape(1, 1, 4)


def from_pieces(received):
    pieces = received.astype(jnp.float32)
    return jnp.sum(pieces[:, 0:2] + pieces[:, 2:4], axis=0)


def slot_numbers(flat_ids, experts):
    onehot = (flat_ids[:, None] == jnp.arange(experts, dtype=jnp.int32)[None, :]).astype(jnp.int32)
    earlier = jnp.cumsum(onehot, axis=0) - onehot
    return jnp.sum(earlier * onehot, axis=1)


def local(hidden, expert_ids, gate_weights, direction, solution, residual):
    sources = hidden.shape[2]
    capacity = hidden.shape[3]
    hidden_units = hidden.shape[4]
    model_width = direction.shape[1]
    tok_rows = expert_ids.shape[1]
    top_count = expert_ids.shape[2]
    experts = lax.axis_size(EXPERT)
    replicas = lax.axis_size(DP)
    shard_rows = model_width // replicas
    norm_scale = 1.0 / (replicas * tok_rows)
    flat_ids = expert_ids.reshape(tok_rows * top_count)
    position = flat_ids * capacity + slot_numbers(flat_ids, experts)
    cached = hidden.reshape(sources * capacity, hidden_units)
    vector = direction.reshape(model_width, hidden_units)
    offset = lax.axis_index(DP) * shard_rows
    own_rows = lax.dynamic_slice_in_dim(vector, offset, shard_rows, 0).astype(jnp.float32)
    residual_rows = residual.reshape(shard_rows, hidden_units)
    images = lax.dot_general(
        cached, vector, (((1,), (1,)), ((), ())), preferred_element_type=jnp.float32
    )
    images = images.astype(jnp.bfloat16).reshape(sources, capacity, model_width)
    returned = lax.all_to_all(images, EXPERT, split_axis=0, concat_axis=0, tiled=True)
    selector = (
        position[:, None] == jnp.arange(experts * capacity, dtype=jnp.int32)[None, :]
    ).astype(jnp.bfloat16)
    row_images = lax.dot_general(
        selector,
        returned.reshape(experts * capacity, model_width),
        (((1,), (0,)), ((), ())),
        preferred_element_type=jnp.float32,
    )
    gate_rows = gate_weights.reshape(tok_rows, top_count)
    tangent = jnp.sum(
        gate_rows[:, :, None] * row_images.reshape(tok_rows, top_count, model_width), axis=1
    )
    weighted = (gate_rows[:, :, None] * tangent[:, None, :]).astype(jnp.bfloat16)
    pairs = capacity // 2
    slot_rows = jnp.arange(experts * pairs, dtype=jnp.int32)
    packed = []
    for parity in range(2):
        target = (slot_rows // pairs) * capacity + (slot_rows % pairs) * 2 + parity
        pick = (position[:, None] == target[None, :]).astype(jnp.bfloat16)
        packed.append(
            lax.dot_general(
                pick,
                weighted.reshape(tok_rows * top_count, model_width),
                (((0,), (0,)), ((), ())),
                preferred_element_type=jnp.float32,
            ).astype(jnp.bfloat16)
        )
    outgoing = jnp.concatenate(packed, axis=1).reshape(experts, pairs, 2 * model_width)
    local_curvature = norm_scale * jnp.sum(tangent * tangent) + jnp.sum(own_rows * own_rows)
    local_sums = jnp.stack([local_curvature, jnp.sum(residual_rows * residual_rows)])
    lanes = 128
    carried = jnp.broadcast_to(
        jnp.pad(as_pieces(local_sums), ((0, 0), (0, pairs - 1), (0, lanes - 4))),
        (experts, pairs, lanes),
    )
    payload = jnp.concatenate([outgoing, carried], axis=2)
    arrived_full = lax.all_to_all(payload, EXPERT, split_axis=0, concat_axis=0, tiled=True)
    expert_sums = from_pieces(arrived_full[:, 0, 2 * model_width : 2 * model_width + 4])
    arrived = arrived_full[:, :, : 2 * model_width].reshape(sources, pairs, 2, model_width)
    partial_value = lax.dot_general(
        arrived,
        hidden.reshape(sources, pairs, 2, hidden_units),
        (((0, 1, 2), (0, 1, 2)), ((), ())),
        preferred_element_type=jnp.float32,
    ).astype(jnp.bfloat16)
    extra_rows = 8
    extra = jnp.broadcast_to(
        jnp.pad(as_pieces(expert_sums), ((0, 0), (0, extra_rows - 1), (0, hidden_units - 4))),
        (replicas, extra_rows, hidden_units),
    )
    blocks = jnp.concatenate([split_up(partial_value, 0, replicas), extra], axis=1)
    exchanged = lax.all_to_all(blocks, DP, 0, 0, tiled=True)
    summed = jnp.sum(exchanged[:, :shard_rows].astype(jnp.float32), axis=0)
    totals = from_pieces(exchanged[:, shard_rows, 0:4])
    product = summed * norm_scale + own_rows
    step_size = totals[1] / totals[0]
    new_solution = solution + step_size * own_rows[None]
    new_residual = residual - step_size * product[None]
    return (new_solution, new_residual)


def solution(mesh):
    torus = Mesh(mesh.devices.reshape(32, 2, 4, 4), ("expert_0", "expert_1", "dp_0", "dp_1"))
    return jax.shard_map(
        local,
        mesh=torus,
        in_specs=(
            P(DP, EXPERT, None, None, None),
            P(DP, EXPERT, None),
            P(DP, EXPERT, None),
            P(EXPERT, None, None),
            P(EXPERT, DP, None),
            P(EXPERT, DP, None),
        ),
        out_specs=(P(EXPERT, DP, None), P(EXPERT, DP, None)),
        check_vma=False,
    )
```

```python
import functools

import jax
import jax.numpy as jnp
from jax import lax
from jax.sharding import Mesh
from jax.sharding import PartitionSpec as P

EXPERT = ("expert_0", "expert_1")
DP = ("dp_0", "dp_1")
EXPERT_DP = ("expert_0", "expert_1", "dp_0", "dp_1")


def over_axes(value, axes):
    return functools.reduce(lax.psum, axes, value)


def split_up(value, dim, count):
    before, after = (value.shape[:dim], value.shape[dim + 1 :])
    return jnp.moveaxis(value.reshape(*before, count, -1, *after), dim, 0)


def sent_and_summed(value, axis, dim):
    count = lax.axis_size(axis)
    blocks = lax.all_to_all(split_up(value, dim, count), axis, 0, 0, tiled=True)
    return jnp.sum(blocks.astype(jnp.float32), axis=0)


def as_pieces(values):
    high = lax.reduce_precision(values, exponent_bits=8, mantissa_bits=7)
    low = (values - high).astype(jnp.bfloat16)
    return jnp.concatenate([high.astype(jnp.bfloat16), low]).reshape(1, 1, 4)


def from_pieces(received):
    pieces = received.astype(jnp.float32)
    return jnp.sum(pieces[:, 0:2] + pieces[:, 2:4], axis=0)


def slot_numbers(flat_ids, experts):
    onehot = (flat_ids[:, None] == jnp.arange(experts, dtype=jnp.int32)[None, :]).astype(jnp.int32)
    earlier = jnp.cumsum(onehot, axis=0) - onehot
    return jnp.sum(earlier * onehot, axis=1)


def local(hidden, expert_ids, gate_weights, direction, solution, residual):
    sources = hidden.shape[2]
    capacity = hidden.shape[3]
    hidden_units = hidden.shape[4]
    model_width = direction.shape[1]
    tok_rows = expert_ids.shape[1]
    top_count = expert_ids.shape[2]
    experts = lax.axis_size(EXPERT)
    replicas = lax.axis_size(DP)
    shard_rows = model_width // replicas
    norm_scale = 1.0 / (replicas * tok_rows)
    flat_ids = expert_ids.reshape(tok_rows * top_count)
    position = flat_ids * capacity + slot_numbers(flat_ids, experts)
    cached = hidden.reshape(sources * capacity, hidden_units)
    vector = direction.reshape(model_width, hidden_units)
    offset = lax.axis_index(DP) * shard_rows
    own_rows = lax.dynamic_slice_in_dim(vector, offset, shard_rows, 0).astype(jnp.float32)
    residual_rows = residual.reshape(shard_rows, hidden_units)
    images = lax.dot_general(
        cached, vector, (((1,), (1,)), ((), ())), preferred_element_type=jnp.float32
    )
    images = images.astype(jnp.bfloat16).reshape(sources, capacity, model_width)
    returned = lax.all_to_all(images, EXPERT, split_axis=0, concat_axis=0, tiled=True)
    selector = (
        position[:, None] == jnp.arange(experts * capacity, dtype=jnp.int32)[None, :]
    ).astype(jnp.bfloat16)
    gate_rows = gate_weights.reshape(tok_rows, top_count)
    gate_select = jnp.sum(
        selector.astype(jnp.float32).reshape(tok_rows, top_count, experts * capacity)
        * gate_rows[:, :, None],
        axis=1,
    )
    tangent = lax.dot_general(
        gate_select,
        returned.reshape(experts * capacity, model_width).astype(jnp.float32),
        (((1,), (0,)), ((), ())),
        precision=lax.Precision.HIGHEST,
        preferred_element_type=jnp.float32,
    )
    weighted = (gate_rows[:, :, None] * tangent[:, None, :]).astype(jnp.bfloat16)
    outgoing = lax.dot_general(
        selector,
        weighted.reshape(tok_rows * top_count, model_width),
        (((0,), (0,)), ((), ())),
        preferred_element_type=jnp.float32,
    ).astype(jnp.bfloat16)
    local_curvature = norm_scale * jnp.sum(tangent * tangent) + jnp.sum(own_rows * own_rows)
    local_sums = jnp.stack([local_curvature, jnp.sum(residual_rows * residual_rows)])
    lanes = 128
    carried = jnp.broadcast_to(
        jnp.pad(as_pieces(local_sums), ((0, 0), (0, capacity - 1), (0, lanes - 4))),
        (experts, capacity, lanes),
    )
    payload = jnp.concatenate([outgoing.reshape(experts, capacity, model_width), carried], axis=2)
    arrived_full = lax.all_to_all(payload, EXPERT, split_axis=0, concat_axis=0, tiled=True)
    expert_sums = from_pieces(arrived_full[:, 0, model_width : model_width + 4])
    arrived = arrived_full[:, :, :model_width].reshape(sources * capacity, model_width)
    partial_value = lax.dot_general(
        arrived, cached, (((0,), (0,)), ((), ())), preferred_element_type=jnp.float32
    ).astype(jnp.bfloat16)
    extra_rows = 8
    extra = jnp.broadcast_to(
        jnp.pad(as_pieces(expert_sums), ((0, 0), (0, extra_rows - 1), (0, hidden_units - 4))),
        (replicas, extra_rows, hidden_units),
    )
    blocks = jnp.concatenate([split_up(partial_value, 0, replicas), extra], axis=1)
    exchanged = lax.all_to_all(blocks, DP, 0, 0, tiled=True)
    summed = jnp.sum(exchanged[:, :shard_rows].astype(jnp.float32), axis=0)
    totals = from_pieces(exchanged[:, shard_rows, 0:4])
    product = summed * norm_scale + own_rows
    step_size = totals[1] / totals[0]
    new_solution = solution + step_size * own_rows[None]
    new_residual = residual - step_size * product[None]
    return (new_solution, new_residual)


def solution(mesh):
    torus = Mesh(mesh.devices.reshape(32, 2, 4, 4), ("expert_0", "expert_1", "dp_0", "dp_1"))
    return jax.shard_map(
        local,
        mesh=torus,
        in_specs=(
            P(DP, EXPERT, None, None, None),
            P(DP, EXPERT, None),
            P(DP, EXPERT, None),
            P(EXPERT, None, None),
            P(EXPERT, DP, None),
            P(EXPERT, DP, None),
        ),
        out_specs=(P(EXPERT, DP, None), P(EXPERT, DP, None)),
        check_vma=False,
    )
```
